128 devices in a mesh: row: 4 (over z), col: 32 (over y, x, core).
Axes of the slice: x: 4, y: 4, z: 4, core: 2. Of those that a mesh axis runs over, the one named last changes fastest.
Arguments:
- pooled: bfloat16 [49152, 1024], P(('row', 'col')), may hold values from -6 to 6
- enc_weight: bfloat16 [1024, 1024], replicated, may hold values from -0.1875 to 0.1875
- norm_gain: float32 [1024], replicated, may hold values from 0.1 to 1.9
- shortlist: int32 [49152, 16], P(('row', 'col')), may hold values from 0 to 1535, all different within a row; in each aligned block of 384 rows (0 to 383, 384 to 767, ...) at most 6 rows name the same one
- positives: int32 [49152, 8], P(('row', 'col')), may hold values from 0 to 4095
- label_weight: bfloat16 [256, 1536, 1024], P(None, ('row', 'col')), may hold values from -0.1875 to 0.1875
Outputs:
- query_grad: float32 [49152, 1024], P(('row', 'col'))
- weight_grad: float32 [256, 1536, 1024], P(None, ('row', 'col'))
The draws below stay inside these ranges and needn't reach their ends.
Inputs may be any that keep to these rules, and one draw needn't show every extreme that they name: `shortlist`: the 16 clusters of a query differ. Among the 384 queries of one device (aligned blocks of rows) no cluster is named more than 6 times, a bound that some block reaches. Every cluster is named by some query. Cluster c is held by the device of index c // 12 along row+col.
All inputs are finite; a program needn't handle non-finite values.
Results may differ from the reference program's by a relative error of at most 0.0038.
Values may be sent and summed in bfloat16 or wider, within the bound.
No kernel may reach another device: no remote copies, remote signals or barrier semaphores. Data moves between devices by JAX's collectives and lax.ppermute only.
A program may use at most 256 MiB of HBM per device.

```python
import math
import jax
import jax.numpy as jnp
import numpy as np
from jax import lax

D = 1024
LBL = 256
K = 16
P_SIZE = 8
CAP = 6
CLUSTERS = 1536
Q_DEV = 384
QUERIES = 49152
N_ROW = 4
N_COL = 32


def place_ends(drawn, key, least, high):
    longest = drawn.shape.index(max(drawn.shape))
    spots = []
    for shift in (0, 1):
        where = [jax.random.randint(jax.random.fold_in(key, axis), (), 0, length) for axis, length in enumerate(drawn.shape)]
        where[longest] = (where[longest] + shift) % drawn.shape[longest]
        spots.append(tuple(where))
    return drawn.at[spots[0]].set(least).at[spots[1]].set(high)


def level_of(own_key, shape, cuts, low, high):
    def one(dim, parts):
        draws = jax.random.uniform(jax.random.fold_in(jax.random.fold_in(own_key, 6), dim), (parts,), jnp.float32, low / len(cuts), high / len(cuts))
        return jnp.repeat(jnp.exp(draws), shape[dim] // parts).reshape((-1,) + (1,) * (len(shape) - dim - 1))

    level = one(*cuts[0])
    for cut in cuts[1:]:
        level = level * one(*cut)
    return level


def shared_out(own_key, own, number, rows, count, top, bound, slope):
    order = jax.random.permutation(own_key, count)
    heavy_load, ordinary = shares(count, rows * top, bound, slope, True), shares(count, rows * top, bound, slope, False)
    places = jnp.arange(count)

    def named(tallies, offset_by):
        used = int((tallies > 0).sum())
        fixed = max(1, used // 4)
        passed = fixed + (places - fixed + offset_by * (used - fixed)) % max(1, count - fixed)
        return jnp.zeros((count,), jnp.int32).at[order[jnp.where(places < fixed, places, passed)]].set(jnp.asarray(tallies, jnp.int32))

    tallies = jnp.where(number % 4 == 0, named(heavy_load, number // 4), named(ordinary, number - number // 4 - 1))
    mixed = jax.random.permutation(jax.random.fold_in(own, 3), count)
    giver, receiver = mixed[0:count // 2 * 2:2], mixed[1:count // 2 * 2:2]
    room = jnp.minimum(tallies[giver] - 1, bound - tallies[receiver]) // 2
    room = jnp.where((giver == order[0]) | (receiver == order[0]) | (tallies[receiver] == 0), 0, jnp.maximum(room, 0))
    passed = jax.random.randint(jax.random.fold_in(own, 4), (count // 2,), 0, 1 << 20) % (room + 1)
    tallies = tallies.at[giver].add(-passed).at[receiver].add(passed)
    items = jnp.searchsorted(jnp.cumsum(tallies), jnp.arange(rows * top), side="right").astype(jnp.int32)
    grid = items.reshape(top, rows).T
    grid = grid[jax.random.permutation(jax.random.fold_in(own, 1), rows)]
    offset_by = jax.random.randint(jax.random.fold_in(own, 2), (rows, 1), 0, top)
    return jnp.take_along_axis(grid, (jnp.arange(top)[None, :] + offset_by) % top, axis=1)


def shares(count, total, reach, lean, full):
    portions = [(1 << 20) // math.isqrt(grade ** lean) + 1 for grade in range(1, count + 1)]
    largest = reach if full else min(reach, max(-(-total // count), total * portions[0] // sum(portions)))
    least = 1 if total - largest >= count - 1 else 0
    holding, spare = [largest] + [least] * (count - 1), total - largest - least * (count - 1)
    while spare > 0:
        candidates = [i for i in range(1, count) if holding[i] < largest] or [i for i in range(1, count) if holding[i] < reach]
        pool, left = sum([portions[i] for i in candidates]), spare
        for i in candidates:
            addition = min(reach - holding[i], max(1, left * portions[i] // pool), spare)
            holding[i] = holding[i] + addition
            spare = spare - addition
    return np.array(holding)


def scatter_about(key, shape, deviation, most, pieces=(), kind=jnp.bfloat16):
    gain = level_of(key, shape, pieces, -0.22, 0.18) if pieces else 1.0
    entries = jax.random.normal(key, shape, jnp.float32) * deviation * gain
    return jnp.minimum(jnp.maximum(entries, -most), most).astype(kind)


def setup_inputs(seed: int = 0) -> dict:
    streams_of = jax.random.split(jax.random.key(seed), 7)
    pooled = scatter_about(streams_of[0], (QUERIES, D), 1.0, 6.0, ((0, 128),))
    enc_weight = scatter_about(streams_of[1], (D, D), D ** -0.5, 0.1875)
    norm_gain = jnp.clip(1.0 + 0.18 * jax.random.normal(streams_of[2], (D,), jnp.float32), 0.1, 1.9)
    shortlist_keys = jax.random.split(jax.random.fold_in(streams_of[3], 1), QUERIES // Q_DEV)
    shortlist_turns = jax.random.permutation(jax.random.fold_in(streams_of[3], 3), QUERIES // Q_DEV)
    shortlist = jax.vmap(lambda own, number: shared_out(jax.random.fold_in(streams_of[3], 2), own, number, Q_DEV, CLUSTERS, K, CAP, 2))(shortlist_keys, shortlist_turns).reshape((QUERIES, K))
    positives = place_ends(jax.random.randint(streams_of[4], (QUERIES, P_SIZE), 0, K * LBL), jax.random.fold_in(streams_of[4], 1), 0, (K * LBL) - 1).astype(jnp.int32)
    label_weight = scatter_about(streams_of[5], (LBL, CLUSTERS, D), D ** -0.5, 0.1875, ((1, 128),))
    return dict(pooled=pooled, enc_weight=enc_weight, norm_gain=norm_gain, shortlist=shortlist, positives=positives, label_weight=label_weight)


def encode(pooled, enc_weight, norm_gain):
    projected = jnp.dot(pooled, enc_weight, preferred_element_type=jnp.float32)
    average = lax.optimization_barrier(jnp.mean(projected, axis=-1, keepdims=True))
    centred = projected - average
    spread = lax.optimization_barrier(jnp.mean(centred * centred, axis=-1, keepdims=True))
    return (centred * lax.rsqrt(spread + 1e-05) * norm_gain).astype(jnp.bfloat16)

def slot_ranks(cluster_ids):
    position = jnp.arange(cluster_ids.shape[0], dtype=jnp.int32)
    same = cluster_ids[:, None] == cluster_ids[None, :]
    earlier = position[:, None] > position[None, :]
    return lax.optimization_barrier(jnp.sum((same & earlier).astype(jnp.int32), axis=1)).astype(jnp.int32)

def reference(pooled, enc_weight, norm_gain, shortlist, positives, label_weight):
    queries = encode(pooled, enc_weight, norm_gain)
    devices = N_ROW * N_COL
    cluster_ids = shortlist.reshape(devices, Q_DEV * K).astype(jnp.int32)
    slot_rank = lax.map(slot_ranks, cluster_ids)
    source = jnp.broadcast_to(jnp.arange(devices, dtype=jnp.int32)[:, None], cluster_ids.shape)
    row_number = jnp.arange(QUERIES * K, dtype=jnp.int32).reshape(devices, Q_DEV * K)
    slot_row = jnp.full((CLUSTERS, devices, CAP), -1, jnp.int32).at[cluster_ids, source, slot_rank].set(row_number)
    offsets = positives[:, None, :] - (jnp.arange(K, dtype=jnp.int32) * LBL)[None, :, None]
    inside = (offsets >= 0) & (offsets < LBL)
    local_positive = jnp.where(inside, offsets, -1).astype(jnp.int32).reshape(QUERIES * K, P_SIZE)
    labels = jnp.arange(LBL, dtype=jnp.int32)
    by_cluster = jnp.transpose(label_weight, (1, 0, 2))

    def advance(running, inputs):
        weight_block, members = inputs
        occupied = members >= 0
        clamped = jnp.maximum(members, 0)
        owner_rows = jnp.where(occupied[..., None], queries[clamped // K], jnp.zeros((), queries.dtype))
        owner_pos = jnp.where(occupied[..., None], local_positive[clamped], -1)
        scores = jnp.einsum('sxd,jd->sxj', owner_rows.astype(jnp.float32), weight_block.astype(jnp.float32))
        target = jnp.any(owner_pos[..., :, None] == labels, axis=-2)
        signal = (jax.nn.sigmoid(scores) - target.astype(jnp.float32)).astype(jnp.bfloat16)
        block_grad = jnp.einsum('sxj,sxd->jd', signal.astype(jnp.float32), owner_rows.astype(jnp.float32))
        row_grads = jnp.einsum('sxj,jd->sxd', signal.astype(jnp.float32), weight_block.astype(jnp.float32)).astype(jnp.bfloat16)
        row_grads = lax.optimization_barrier(row_grads).astype(jnp.float32)
        running = running.at[clamped // K].add(jnp.where(occupied[..., None], row_grads, jnp.zeros((), jnp.float32)))
        return (running, block_grad)
    start = jnp.zeros((QUERIES, D), jnp.float32)
    query_grad, block_grads = lax.scan(advance, start, (by_cluster, slot_row))
    return (query_grad, jnp.transpose(block_grads, (1, 0, 2)))
```

```python
import jax
import jax.numpy as jnp
from jax import lax
from jax.sharding import PartitionSpec as P

CAP = 6
AXES = ("row", "col")


def encode(pooled, enc_weight, norm_gain):
    projected = jnp.dot(pooled, enc_weight, preferred_element_type=jnp.float32)
    average = jnp.mean(projected, axis=-1, keepdims=True)
    centred = projected - average
    spread = jnp.mean(centred * centred, axis=-1, keepdims=True)
    return (centred * lax.rsqrt(spread + 1e-05) * norm_gain).astype(jnp.bfloat16)


def on_device(pooled, enc_weight, norm_gain, shortlist, positives, label_weight):
    queries = encode(pooled, enc_weight, norm_gain)
    devices = lax.axis_size("row") * lax.axis_size("col")
    query_count, width = queries.shape
    block_labels, local_clusters, _ = label_weight.shape
    shortlist_size = shortlist.shape[1]
    positive_count = positives.shape[1]
    clusters = devices * local_clusters
    slots = clusters * CAP

    cluster_id = jnp.arange(clusters, dtype=jnp.int32)
    hit = shortlist.T[:, None, :] == cluster_id[None, :, None]
    member = jnp.any(hit, axis=0)
    position = jnp.sum(
        jnp.where(hit, jnp.arange(shortlist_size, dtype=jnp.int32)[:, None, None], 0), axis=0
    )
    earlier = (
        jnp.arange(query_count, dtype=jnp.int32)[:, None]
        < jnp.arange(query_count, dtype=jnp.int32)[None, :]
    ).astype(jnp.bfloat16)
    rank = jnp.dot(member.astype(jnp.bfloat16), earlier, preferred_element_type=jnp.float32)
    slot_of = jnp.arange(CAP, dtype=jnp.float32)
    dispatch = member[:, None, :] & (rank[:, None, :] == slot_of[None, :, None])
    dispatch = dispatch.astype(jnp.bfloat16).reshape(slots, query_count)

    outgoing = jnp.dot(dispatch, queries, preferred_element_type=jnp.float32).astype(jnp.bfloat16)
    split = jnp.concatenate([positives // 256, positives % 256], axis=1).astype(jnp.bfloat16)
    gathered = jnp.dot(dispatch, split, preferred_element_type=jnp.float32)
    raw = (gathered[:, :positive_count] * 256 + gathered[:, positive_count:]).astype(jnp.int32)
    picked = dispatch.reshape(clusters, CAP, query_count).astype(jnp.float32)
    slot_k = jnp.sum(picked * position[:, None, :].astype(jnp.float32), axis=2).reshape(slots, 1)
    occupied = jnp.sum(picked, axis=2).reshape(slots, 1) > 0
    offsets = raw - slot_k.astype(jnp.int32) * block_labels
    inside = (offsets >= 0) & (offsets < block_labels) & occupied
    local_positive = jnp.where(inside, offsets, -1).astype(jnp.int32)

    incoming = lax.all_to_all(
        outgoing.reshape(devices, local_clusters, CAP, width),
        AXES, split_axis=0, concat_axis=2, tiled=True,
    ).reshape(local_clusters, devices * CAP, width)
    incoming_pos = lax.all_to_all(
        local_positive.reshape(devices, local_clusters, CAP, positive_count),
        AXES, split_axis=0, concat_axis=2, tiled=True,
    ).reshape(local_clusters, devices * CAP, positive_count)

    scores = jnp.einsum(
        "cnd,jcd->cnj", incoming, label_weight, preferred_element_type=jnp.float32
    )
    labels = jnp.arange(block_labels, dtype=jnp.int32)
    target = jnp.zeros(scores.shape, jnp.bool_)
    for column in range(positive_count):
        target = target | (incoming_pos[..., column : column + 1] == labels)
    signal = (jax.nn.sigmoid(scores) - target.astype(jnp.float32)).astype(jnp.bfloat16)
    weight_grad = jnp.einsum("cnj,cnd->jcd", signal, incoming, preferred_element_type=jnp.float32)
    row_grads = jnp.einsum(
        "cnj,jcd->cnd", signal, label_weight, preferred_element_type=jnp.float32
    ).astype(jnp.bfloat16)
    returned = lax.all_to_all(
        row_grads.reshape(1, local_clusters, devices * CAP, width),
        AXES, split_axis=2, concat_axis=0, tiled=True,
    ).reshape(slots, width)
    query_grad = lax.dot_general(
        dispatch, returned, (((0,), (0,)), ((), ())), preferred_element_type=jnp.float32
    )
    return (query_grad, weight_grad)


def solution(mesh):
    in_specs = (
        P(AXES, None),
        P(),
        P(),
        P(AXES, None),
        P(AXES, None),
        P(None, AXES, None),
    )
    out_specs = (P(AXES, None), P(None, AXES, None))
    return jax.shard_map(
        on_device, mesh=mesh, in_specs=in_specs, out_specs=out_specs, check_vma=False
    )
```

```python
import jax
import jax.numpy as jnp
from jax import lax
from jax.sharding import PartitionSpec as P

CAP = 6
AXES = ("row", "col")


def encode(pooled, enc_weight, norm_gain):
    projected = jnp.dot(pooled, enc_weight, preferred_element_type=jnp.float32)
    average = jnp.mean(projected, axis=-1, keepdims=True)
    centred = projected - average
    spread = jnp.mean(centred * centred, axis=-1, keepdims=True)
    return (centred * lax.rsqrt(spread + 1e-05) * norm_gain).astype(jnp.bfloat16)


def on_device(pooled, enc_weight, norm_gain, shortlist, positives, label_weight):
    queries = encode(pooled, enc_weight, norm_gain)
    devices = lax.axis_size("row") * lax.axis_size("col")
    query_count, width = queries.shape
    block_labels, local_clusters, _ = label_weight.shape
    shortlist_size = shortlist.shape[1]
    positive_count = positives.shape[1]
    clusters = devices * local_clusters
    slots = clusters * CAP

    cluster_id = jnp.arange(clusters, dtype=jnp.int32)
    member = jnp.any(shortlist.T[:, None, :] == cluster_id[None, :, None], axis=0)
    earlier = (
        jnp.arange(query_count, dtype=jnp.int32)[:, None]
        < jnp.arange(query_count, dtype=jnp.int32)[None, :]
    ).astype(jnp.bfloat16)
    rank = jnp.dot(member.astype(jnp.bfloat16), earlier, preferred_element_type=jnp.float32)
    level = jnp.where(member, rank, float(CAP + 1)).astype(jnp.bfloat16)
    slot_rank = (jnp.arange(slots, dtype=jnp.int32) % CAP).astype(jnp.bfloat16)
    dispatch = (jnp.repeat(level, CAP, axis=0) == slot_rank[:, None]).astype(jnp.bfloat16)

    outgoing = jnp.dot(dispatch, queries, preferred_element_type=jnp.float32).astype(jnp.bfloat16)
    parts = jnp.concatenate(
        [shortlist // 256, shortlist % 256, positives // 256, positives % 256,
         jnp.ones((query_count, 1), jnp.int32)],
        axis=1,
    ).astype(jnp.bfloat16)
    gathered = jnp.dot(dispatch, parts, preferred_element_type=jnp.float32)
    k_hi = gathered[:, :shortlist_size]
    k_lo = gathered[:, shortlist_size : 2 * shortlist_size]
    p_base = 2 * shortlist_size
    slot_list = (k_hi * 256 + k_lo).astype(jnp.int32)
    raw = (
        gathered[:, p_base : p_base + positive_count] * 256
        + gathered[:, p_base + positive_count : p_base + 2 * positive_count]
    ).astype(jnp.int32)
    occupied = gathered[:, p_base + 2 * positive_count :] > 0.5
    slot_cluster = jnp.arange(slots, dtype=jnp.int32)[:, None] // CAP
    slot_k = jnp.sum(
        jnp.where(slot_list == slot_cluster, jnp.arange(shortlist_size, dtype=jnp.int32), 0),
        axis=1, keepdims=True,
    )
    offsets = raw - slot_k * block_labels
    inside = (offsets >= 0) & (offsets < block_labels) & occupied
    local_positive = jnp.where(inside, offsets, -1).astype(jnp.int32)

    per_dst = local_clusters * CAP
    incoming = lax.all_to_all(
        outgoing.reshape(devices, per_dst, width), AXES, split_axis=0, concat_axis=0, tiled=True
    )
    incoming = (
        incoming.reshape(devices, local_clusters, CAP, width)
        .transpose(1, 0, 2, 3)
        .reshape(local_clusters, devices * CAP, width)
    )
    incoming_pos = lax.all_to_all(
        local_positive.reshape(devices, per_dst, positive_count),
        AXES, split_axis=0, concat_axis=0, tiled=True,
    )
    incoming_pos = (
        incoming_pos.reshape(devices, local_clusters, CAP, positive_count)
        .transpose(1, 0, 2, 3)
        .reshape(local_clusters, devices * CAP, positive_count)
    )

    scores = jnp.einsum(
        "cnd,jcd->cnj", incoming, label_weight, preferred_element_type=jnp.float32
    )
    labels = jnp.arange(block_labels, dtype=jnp.int32)
    target = jnp.zeros(scores.shape, jnp.bool_)
    for column in range(positive_count):
        target = target | (incoming_pos[..., column : column + 1] == labels)
    signal = (jax.nn.sigmoid(scores) - target.astype(jnp.float32)).astype(jnp.bfloat16)
    weight_grad = jnp.einsum("cnj,cnd->jcd", signal, incoming, preferred_element_type=jnp.float32)
    row_grads = jnp.einsum(
        "cnj,jcd->cnd", signal, label_weight, preferred_element_type=jnp.float32
    ).astype(jnp.bfloat16)
    row_grads = (
        row_grads.reshape(local_clusters, devices, CAP, width)
        .transpose(1, 0, 2, 3)
        .reshape(devices, per_dst, width)
    )
    returned = lax.all_to_all(
        row_grads, AXES, split_axis=0, concat_axis=0, tiled=True
    ).reshape(slots, width)
    query_grad = lax.dot_general(
        dispatch, returned, (((0,), (0,)), ((), ())), preferred_element_type=jnp.float32
    )
    return (query_grad, weight_grad)


def solution(mesh):
    in_specs = (
        P(AXES, None),
        P(),
        P(),
        P(AXES, None),
        P(AXES, None),
        P(None, AXES, None),
    )
    out_specs = (P(AXES, None), P(None, AXES, None))
    return jax.shard_map(
        on_device, mesh=mesh, in_specs=in_specs, out_specs=out_specs, check_vma=False
    )
```

```python
import jax
import jax.numpy as jnp
from jax import lax
from jax.sharding import PartitionSpec as P
from jax.experimental import pallas as pl
from jax.experimental.pallas import tpu as pltpu

CAP = 6
AXES = ("row", "col")


def encode(pooled, enc_weight, norm_gain):
    projected = jnp.dot(pooled, enc_weight, preferred_element_type=jnp.float32)
    average = jnp.mean(projected, axis=-1, keepdims=True)
    centred = projected - average
    spread = jnp.mean(centred * centred, axis=-1, keepdims=True)
    return (centred * lax.rsqrt(spread + 1e-05) * norm_gain).astype(jnp.bfloat16)


def cluster_kernel(incoming_ref, positive_ref, weight_ref, grad_ref, rows_ref):
    block = weight_ref[0]
    x = incoming_ref[...]
    scores = lax.dot_general(
        x, block, (((1,), (1,)), ((), ())), preferred_element_type=jnp.float32
    )
    labels = lax.broadcasted_iota(jnp.int32, (1, block.shape[0]), 1)
    marks = positive_ref[...]
    target = marks[:, 0:1] == labels
    for column in range(1, marks.shape[1]):
        target = target | (marks[:, column : column + 1] == labels)
    signal = (jax.nn.sigmoid(scores) - target.astype(jnp.float32)).astype(jnp.bfloat16)
    grad_ref[0] = lax.dot_general(
        signal, x, (((0,), (0,)), ((), ())), preferred_element_type=jnp.float32
    )
    rows_ref[...] = jnp.dot(signal, block, preferred_element_type=jnp.float32).astype(jnp.bfloat16)


def on_device(pooled, enc_weight, norm_gain, shortlist, positives, label_weight):
    queries = encode(pooled, enc_weight, norm_gain)
    devices = lax.axis_size("row") * lax.axis_size("col")
    query_count, width = queries.shape
    block_labels, local_clusters, _ = label_weight.shape
    shortlist_size = shortlist.shape[1]
    positive_count = positives.shape[1]
    clusters = devices * local_clusters
    slots = clusters * CAP
    per_dst = local_clusters * CAP

    local_of = jnp.arange(local_clusters, dtype=jnp.int32)[:, None]
    device_of = jnp.arange(devices, dtype=jnp.int32)[None, :]
    cluster_id = (device_of * local_clusters + local_of).reshape(clusters)
    member = jnp.any(shortlist.T[:, None, :] == cluster_id[None, :, None], axis=0)
    earlier = (
        jnp.arange(query_count, dtype=jnp.int32)[:, None]
        < jnp.arange(query_count, dtype=jnp.int32)[None, :]
    ).astype(jnp.bfloat16)
    rank = jnp.dot(member.astype(jnp.bfloat16), earlier, preferred_element_type=jnp.float32)
    level = jnp.where(member, rank, float(CAP + 1)).astype(jnp.bfloat16)
    level = level.reshape(local_clusters, 1, devices, query_count)
    slot_rank = jnp.arange(CAP, dtype=jnp.int32).astype(jnp.bfloat16)[None, :, None, None]
    dispatch = (level == slot_rank).astype(jnp.bfloat16).reshape(slots, query_count)

    outgoing = jnp.dot(dispatch, queries, preferred_element_type=jnp.float32).astype(jnp.bfloat16)
    parts = jnp.concatenate(
        [shortlist // 256, shortlist % 256, positives // 256, positives % 256,
         jnp.ones((query_count, 1), jnp.int32)],
        axis=1,
    ).astype(jnp.bfloat16)
    gathered = jnp.dot(dispatch, parts, preferred_element_type=jnp.float32)
    k_hi = gathered[:, :shortlist_size]
    k_lo = gathered[:, shortlist_size : 2 * shortlist_size]
    p_base = 2 * shortlist_size
    slot_list = (k_hi * 256 + k_lo).astype(jnp.int32)
    raw = (
        gathered[:, p_base : p_base + positive_count] * 256
        + gathered[:, p_base + positive_count : p_base + 2 * positive_count]
    ).astype(jnp.int32)
    occupied = gathered[:, p_base + 2 * positive_count :] > 0.5
    row = jnp.arange(slots, dtype=jnp.int32)[:, None]
    slot_cluster = (row % devices) * local_clusters + row // (CAP * devices)
    slot_k = jnp.sum(
        jnp.where(slot_list == slot_cluster, jnp.arange(shortlist_size, dtype=jnp.int32), 0),
        axis=1, keepdims=True,
    )
    offsets = raw - slot_k * block_labels
    inside = (offsets >= 0) & (offsets < block_labels) & occupied
    local_positive = jnp.where(inside, offsets, -1).astype(jnp.int32)

    incoming = lax.all_to_all(
        outgoing.reshape(per_dst, devices, width), AXES, split_axis=1, concat_axis=1, tiled=True
    ).reshape(slots, width)
    incoming_pos = lax.all_to_all(
        local_positive.reshape(per_dst, devices, positive_count),
        AXES, split_axis=1, concat_axis=1, tiled=True,
    ).reshape(slots, positive_count)
    by_cluster = jnp.transpose(label_weight, (1, 0, 2))
    rows_per_cluster = CAP * devices
    grad, row_grads = pl.pallas_call(
        cluster_kernel,
        grid=(local_clusters,),
        in_specs=[
            pl.BlockSpec((rows_per_cluster, width), lambda c: (c, 0)),
            pl.BlockSpec((rows_per_cluster, positive_count), lambda c: (c, 0)),
            pl.BlockSpec((1, block_labels, width), lambda c: (c, 0, 0)),
        ],
        out_specs=[
            pl.BlockSpec((1, block_labels, width), lambda c: (c, 0, 0)),
            pl.BlockSpec((rows_per_cluster, width), lambda c: (c, 0)),
        ],
        out_shape=[
            jax.ShapeDtypeStruct((local_clusters, block_labels, width), jnp.float32),
            jax.ShapeDtypeStruct((slots, width), jnp.bfloat16),
        ],
        compiler_params=pltpu.CompilerParams(vmem_limit_bytes=48 * 1024 * 1024),
        cost_estimate=pl.CostEstimate(
            flops=6 * slots * block_labels * width,
            transcendentals=slots * block_labels,
            bytes_accessed=2 * slots * width * 2 + local_clusters * block_labels * width * 6,
        ),
    )(incoming, incoming_pos, by_cluster)
    weight_grad = jnp.transpose(grad, (1, 0, 2))
    returned = lax.all_to_all(
        row_grads.reshape(per_dst, devices, width), AXES, split_axis=1, concat_axis=1, tiled=True
    ).reshape(slots, width)
    query_grad = lax.dot_general(
        dispatch, returned, (((0,), (0,)), ((), ())), preferred_element_type=jnp.float32
    )
    return (query_grad, weight_grad)


def solution(mesh):
    in_specs = (
        P(AXES, None),
        P(),
        P(),
        P(AXES, None),
        P(AXES, None),
        P(None, AXES, None),
    )
    out_specs = (P(AXES, None), P(None, AXES, None))
    return jax.shard_map(
        on_device, mesh=mesh, in_specs=in_specs, out_specs=out_specs, check_vma=False
    )
```

```python
import jax
import jax.numpy as jnp
from jax import lax
from jax.sharding import PartitionSpec as P
from jax.experimental import pallas as pl
from jax.experimental.pallas import tpu as pltpu

CAP = 6
AXES = ("row", "col")


def encode(pooled, enc_weight, norm_gain):
    projected = jnp.dot(pooled, enc_weight, preferred_element_type=jnp.float32)
    average = jnp.mean(projected, axis=-1, keepdims=True)
    centred = projected - average
    spread = jnp.mean(centred * centred, axis=-1, keepdims=True)
    return (centred * lax.rsqrt(spread + 1e-05) * norm_gain).astype(jnp.bfloat16)


def cluster_kernel(incoming_ref, positive_ref, weight_ref, grad_ref, rows_ref):
    block = weight_ref[0]
    x = incoming_ref[...]
    scores = lax.dot_general(
        x, block, (((1,), (1,)), ((), ())), preferred_element_type=jnp.float32
    )
    labels = lax.broadcasted_iota(jnp.int32, (1, block.shape[0]), 1)
    marks = positive_ref[...]
    target = marks[:, 0:1] == labels
    for column in range(1, marks.shape[1]):
        target = target | (marks[:, column : column + 1] == labels)
    signal = (jax.nn.sigmoid(scores) - target.astype(jnp.float32)).astype(jnp.bfloat16)
    grad_ref[0] = lax.dot_general(
        signal, x, (((0,), (0,)), ((), ())), preferred_element_type=jnp.float32
    )
    rows_ref[...] = jnp.dot(signal, block, preferred_element_type=jnp.float32).astype(jnp.bfloat16)


def on_device(pooled, enc_weight, norm_gain, shortlist, positives, label_weight):
    queries = encode(pooled, enc_weight, norm_gain)
    devices = lax.axis_size("row") * lax.axis_size("col")
    query_count, width = queries.shape
    block_labels, local_clusters, _ = label_weight.shape
    shortlist_size = shortlist.shape[1]
    positive_count = positives.shape[1]
    clusters = devices * local_clusters
    slots = clusters * CAP
    per_dst = local_clusters * CAP

    local_of = jnp.arange(local_clusters, dtype=jnp.int32)[:, None]
    device_of = jnp.arange(devices, dtype=jnp.int32)[None, :]
    cluster_id = (device_of * local_clusters + local_of).reshape(clusters)
    member = jnp.any(shortlist.T[:, None, :] == cluster_id[None, :, None], axis=0)
    earlier = (
        jnp.arange(query_count, dtype=jnp.int32)[:, None]
        < jnp.arange(query_count, dtype=jnp.int32)[None, :]
    ).astype(jnp.bfloat16)
    rank = jnp.dot(member.astype(jnp.bfloat16), earlier, preferred_element_type=jnp.float32)
    level = jnp.where(member, rank, float(CAP + 1)).astype(jnp.bfloat16)
    level = level.reshape(local_clusters, 1, devices, query_count)
    slot_rank = jnp.arange(CAP, dtype=jnp.int32).astype(jnp.bfloat16)[None, :, None, None]
    dispatch = (
        (level == slot_rank).astype(jnp.bfloat16).transpose(2, 0, 1, 3).reshape(slots, query_count)
    )

    outgoing = jnp.dot(dispatch, queries, preferred_element_type=jnp.float32).astype(jnp.bfloat16)
    parts = jnp.concatenate(
        [shortlist // 256, shortlist % 256, positives // 256, positives % 256,
         jnp.ones((query_count, 1), jnp.int32)],
        axis=1,
    ).astype(jnp.bfloat16)
    gathered = jnp.dot(dispatch, parts, preferred_element_type=jnp.float32)
    k_hi = gathered[:, :shortlist_size]
    k_lo = gathered[:, shortlist_size : 2 * shortlist_size]
    p_base = 2 * shortlist_size
    slot_list = (k_hi * 256 + k_lo).astype(jnp.int32)
    raw = (
        gathered[:, p_base : p_base + positive_count] * 256
        + gathered[:, p_base + positive_count : p_base + 2 * positive_count]
    ).astype(jnp.int32)
    occupied = gathered[:, p_base + 2 * positive_count :] > 0.5
    row = jnp.arange(slots, dtype=jnp.int32)[:, None]
    slot_cluster = row // CAP
    slot_k = jnp.sum(
        jnp.where(slot_list == slot_cluster, jnp.arange(shortlist_size, dtype=jnp.int32), 0),
        axis=1, keepdims=True,
    )
    offsets = raw - slot_k * block_labels
    inside = (offsets >= 0) & (offsets < block_labels) & occupied
    local_positive = jnp.where(inside, offsets, -1).astype(jnp.int32)

    incoming = lax.all_to_all(
        outgoing.reshape(devices, per_dst, width), AXES, split_axis=0, concat_axis=0, tiled=True
    ).transpose(1, 0, 2).reshape(slots, width)
    incoming_pos = lax.all_to_all(
        local_positive.reshape(devices, per_dst, positive_count),
        AXES, split_axis=0, concat_axis=0, tiled=True,
    ).transpose(1, 0, 2).reshape(slots, positive_count)
    by_cluster = jnp.transpose(label_weight, (1, 0, 2))
    rows_per_cluster = CAP * devices
    grad, row_grads = pl.pallas_call(
        cluster_kernel,
        grid=(local_clusters,),
        in_specs=[
            pl.BlockSpec((rows_per_cluster, width), lambda c: (c, 0)),
            pl.BlockSpec((rows_per_cluster, positive_count), lambda c: (c, 0)),
            pl.BlockSpec((1, block_labels, width), lambda c: (c, 0, 0)),
        ],
        out_specs=[
            pl.BlockSpec((1, block_labels, width), lambda c: (c, 0, 0)),
            pl.BlockSpec((rows_per_cluster, width), lambda c: (c, 0)),
        ],
        out_shape=[
            jax.ShapeDtypeStruct((local_clusters, block_labels, width), jnp.float32),
            jax.ShapeDtypeStruct((slots, width), jnp.bfloat16),
        ],
        compiler_params=pltpu.CompilerParams(vmem_limit_bytes=48 * 1024 * 1024),
        cost_estimate=pl.CostEstimate(
            flops=6 * slots * block_labels * width,
            transcendentals=slots * block_labels,
            bytes_accessed=2 * slots * width * 2 + local_clusters * block_labels * width * 6,
        ),
    )(incoming, incoming_pos, by_cluster)
    weight_grad = jnp.transpose(grad, (1, 0, 2))
    row_grads = row_grads.reshape(per_dst, devices, width).transpose(1, 0, 2)
    returned = lax.all_to_all(
        row_grads, AXES, split_axis=0, concat_axis=0, tiled=True
    ).reshape(slots, width)
    query_grad = lax.dot_general(
        dispatch, returned, (((0,), (0,)), ((), ())), preferred_element_type=jnp.float32
    )
    return (query_grad, weight_grad)


def solution(mesh):
    in_specs = (
        P(AXES, None),
        P(),
        P(),
        P(AXES, None),
        P(AXES, None),
        P(None, AXES, None),
    )
    out_specs = (P(AXES, None), P(None, AXES, None))
    return jax.shard_map(
        on_device, mesh=mesh, in_specs=in_specs, out_specs=out_specs, check_vma=False
    )
```

```python
import jax
import jax.numpy as jnp
from jax import lax
from jax.sharding import PartitionSpec as P
from jax.experimental import pallas as pl
from jax.experimental.pallas import tpu as pltpu

CAP = 6
CHUNKS = (8, 4)
AXES = ("row", "col")


def encode(pooled, enc_weight, norm_gain):
    projected = jnp.dot(pooled, enc_weight, preferred_element_type=jnp.float32)
    average = jnp.mean(projected, axis=-1, keepdims=True)
    centred = projected - average
    spread = jnp.mean(centred * centred, axis=-1, keepdims=True)
    return (centred * lax.rsqrt(spread + 1e-05) * norm_gain).astype(jnp.bfloat16)


def cluster_kernel(incoming_ref, positive_ref, weight_ref, *refs):
    grad_ref, rows_ref = refs[-2:]
    block = weight_ref[0]
    x = incoming_ref[...]
    scores = lax.dot_general(
        x, block, (((1,), (1,)), ((), ())), preferred_element_type=jnp.float32
    )
    labels = lax.broadcasted_iota(jnp.int32, (1, block.shape[0]), 1)
    marks = positive_ref[...]
    target = marks[:, 0:1] == labels
    for column in range(1, marks.shape[1]):
        target = target | (marks[:, column : column + 1] == labels)
    signal = (jax.nn.sigmoid(scores) - target.astype(jnp.float32)).astype(jnp.bfloat16)
    grad_ref[0] = lax.dot_general(
        signal, x, (((0,), (0,)), ((), ())), preferred_element_type=jnp.float32
    )
    rows_ref[...] = jnp.dot(signal, block, preferred_element_type=jnp.float32).astype(jnp.bfloat16)


def on_device(pooled, enc_weight, norm_gain, shortlist, positives, label_weight):
    queries = encode(pooled, enc_weight, norm_gain)
    devices = lax.axis_size("row") * lax.axis_size("col")
    query_count, width = queries.shape
    block_labels, local_clusters, _ = label_weight.shape
    shortlist_size = shortlist.shape[1]
    positive_count = positives.shape[1]
    clusters = devices * local_clusters
    slots = clusters * CAP
    per_dst = local_clusters * CAP

    local_of = jnp.arange(local_clusters, dtype=jnp.int32)[:, None]
    device_of = jnp.arange(devices, dtype=jnp.int32)[None, :]
    cluster_id = (device_of * local_clusters + local_of).reshape(clusters)
    member = jnp.any(shortlist.T[:, None, :] == cluster_id[None, :, None], axis=0)
    earlier = (
        jnp.arange(query_count, dtype=jnp.int32)[:, None]
        < jnp.arange(query_count, dtype=jnp.int32)[None, :]
    ).astype(jnp.bfloat16)
    rank = jnp.dot(member.astype(jnp.bfloat16), earlier, preferred_element_type=jnp.float32)
    level = jnp.where(member, rank, float(CAP + 1)).astype(jnp.bfloat16)
    level = level.reshape(local_clusters, 1, devices, query_count)
    slot_rank = jnp.arange(CAP, dtype=jnp.int32).astype(jnp.bfloat16)[None, :, None, None]
    dispatch = (
        (level == slot_rank).astype(jnp.bfloat16).transpose(2, 0, 1, 3).reshape(slots, query_count)
    )

    parts = jnp.concatenate(
        [shortlist // 256, shortlist % 256, positives // 256, positives % 256,
         jnp.ones((query_count, 1), jnp.int32)],
        axis=1,
    ).astype(jnp.bfloat16)
    gathered = jnp.dot(dispatch, parts, preferred_element_type=jnp.float32)
    k_hi = gathered[:, :shortlist_size]
    k_lo = gathered[:, shortlist_size : 2 * shortlist_size]
    p_base = 2 * shortlist_size
    slot_list = (k_hi * 256 + k_lo).astype(jnp.int32)
    raw = (
        gathered[:, p_base : p_base + positive_count] * 256
        + gathered[:, p_base + positive_count : p_base + 2 * positive_count]
    ).astype(jnp.int32)
    occupied = gathered[:, p_base + 2 * positive_count :] > 0.5
    row = jnp.arange(slots, dtype=jnp.int32)[:, None]
    slot_cluster = row // CAP
    slot_k = jnp.sum(
        jnp.where(slot_list == slot_cluster, jnp.arange(shortlist_size, dtype=jnp.int32), 0),
        axis=1, keepdims=True,
    )
    offsets = raw - slot_k * block_labels
    inside = (offsets >= 0) & (offsets < block_labels) & occupied
    local_positive = jnp.where(inside, offsets, -1).astype(jnp.int32)

    incoming_pos = lax.all_to_all(
        local_positive.reshape(devices, per_dst, positive_count),
        AXES, split_axis=0, concat_axis=0, tiled=True,
    ).transpose(1, 0, 2).reshape(slots, positive_count)
    by_cluster = jnp.transpose(label_weight, (1, 0, 2))
    rows_per_cluster = CAP * devices
    dispatch = dispatch.reshape(devices, per_dst, query_count)
    query_grad = jnp.zeros((query_count, width), jnp.float32)
    grad = None
    first = 0
    for count in CHUNKS:
        rows = count * CAP
        part = dispatch[:, first * CAP : first * CAP + rows, :].reshape(devices * rows, query_count)
        outgoing = jnp.dot(part, queries, preferred_element_type=jnp.float32).astype(jnp.bfloat16)
        incoming = lax.all_to_all(
            outgoing.reshape(devices, rows, width), AXES, split_axis=0, concat_axis=0, tiled=True
        ).transpose(1, 0, 2).reshape(devices * rows, width)
        operands = [incoming, incoming_pos, by_cluster]
        aliases = {}
        if grad is not None:
            operands.append(grad)
            aliases = {3: 0}
        grad, row_grads = pl.pallas_call(
            cluster_kernel,
            grid=(count,),
            in_specs=[
                pl.BlockSpec((rows_per_cluster, width), lambda c: (c, 0)),
                pl.BlockSpec((rows_per_cluster, positive_count), lambda c, f=first: (c + f, 0)),
                pl.BlockSpec((1, block_labels, width), lambda c, f=first: (c + f, 0, 0)),
            ] + ([pl.BlockSpec(memory_space=pl.ANY)] if aliases else []),
            out_specs=[
                pl.BlockSpec((1, block_labels, width), lambda c, f=first: (c + f, 0, 0)),
                pl.BlockSpec((rows_per_cluster, width), lambda c: (c, 0)),
            ],
            out_shape=[
                jax.ShapeDtypeStruct((local_clusters, block_labels, width), jnp.float32),
                jax.ShapeDtypeStruct((devices * rows, width), jnp.bfloat16),
            ],
            input_output_aliases=aliases,
            compiler_params=pltpu.CompilerParams(vmem_limit_bytes=48 * 1024 * 1024),
            cost_estimate=pl.CostEstimate(
                flops=6 * devices * rows * block_labels * width,
                transcendentals=devices * rows * block_labels,
                bytes_accessed=4 * devices * rows * width + count * block_labels * width * 6,
            ),
        )(*operands)
        row_grads = row_grads.reshape(rows, devices, width).transpose(1, 0, 2)
        returned = lax.all_to_all(
            row_grads, AXES, split_axis=0, concat_axis=0, tiled=True
        ).reshape(devices * rows, width)
        query_grad = query_grad + lax.dot_general(
            part, returned, (((0,), (0,)), ((), ())), preferred_element_type=jnp.float32
        )
        first += count
    weight_grad = jnp.transpose(grad, (1, 0, 2))
    return (query_grad, weight_grad)


def solution(mesh):
    in_specs = (
        P(AXES, None),
        P(),
        P(),
        P(AXES, None),
        P(AXES, None),
        P(None, AXES, None),
    )
    out_specs = (P(AXES, None), P(None, AXES, None))
    return jax.shard_map(
        on_device, mesh=mesh, in_specs=in_specs, out_specs=out_specs, check_vma=False
    )
```

```python
import jax
import jax.numpy as jnp
from jax import lax
from jax.sharding import PartitionSpec as P
from jax.experimental import pallas as pl
from jax.experimental.pallas import tpu as pltpu

CAP = 6
CHUNKS = (4, 8)
AXES = ("row", "col")


def encode(pooled, enc_weight, norm_gain):
    projected = jnp.dot(pooled, enc_weight, preferred_element_type=jnp.float32)
    average = jnp.mean(projected, axis=-1, keepdims=True)
    centred = projected - average
    spread = jnp.mean(centred * centred, axis=-1, keepdims=True)
    return (centred * lax.rsqrt(spread + 1e-05) * norm_gain).astype(jnp.bfloat16)


def cluster_kernel(incoming_ref, positive_ref, weight_ref, *refs):
    grad_ref, rows_ref = refs[-2:]
    block = weight_ref[0]
    x = incoming_ref[...]
    scores = lax.dot_general(
        x, block, (((1,), (1,)), ((), ())), preferred_element_type=jnp.float32
    )
    labels = lax.broadcasted_iota(jnp.int32, (1, block.shape[0]), 1)
    marks = positive_ref[...]
    target = marks[:, 0:1] == labels
    for column in range(1, marks.shape[1]):
        target = target | (marks[:, column : column + 1] == labels)
    signal = (jax.nn.sigmoid(scores) - target.astype(jnp.float32)).astype(jnp.bfloat16)
    grad_ref[0] = lax.dot_general(
        signal, x, (((0,), (0,)), ((), ())), preferred_element_type=jnp.float32
    )
    rows_ref[...] = jnp.dot(signal, block, preferred_element_type=jnp.float32).astype(jnp.bfloat16)


def step(pooled, enc_weight, norm_gain, shortlist, positives, label_weight):
    queries = encode(pooled, enc_weight, norm_gain)
    devices = lax.axis_size("row") * lax.axis_size("col")
    query_count, width = queries.shape
    block_labels, local_clusters, _ = label_weight.shape
    shortlist_size = shortlist.shape[1]
    positive_count = positives.shape[1]
    clusters = devices * local_clusters
    slots = clusters * CAP
    per_dst = local_clusters * CAP

    local_of = jnp.arange(local_clusters, dtype=jnp.int32)[:, None]
    device_of = jnp.arange(devices, dtype=jnp.int32)[None, :]
    cluster_id = (device_of * local_clusters + local_of).reshape(clusters)
    member = jnp.any(shortlist.T[:, None, :] == cluster_id[None, :, None], axis=0)
    earlier = (
        jnp.arange(query_count, dtype=jnp.int32)[:, None]
        < jnp.arange(query_count, dtype=jnp.int32)[None, :]
    ).astype(jnp.bfloat16)
    rank = jnp.dot(member.astype(jnp.bfloat16), earlier, preferred_element_type=jnp.float32)
    level = jnp.where(member, rank, float(CAP + 1)).astype(jnp.bfloat16)
    level = level.reshape(local_clusters, 1, devices, query_count)
    slot_rank = jnp.arange(CAP, dtype=jnp.int32).astype(jnp.bfloat16)[None, :, None, None]
    dispatch = (
        (level == slot_rank).astype(jnp.bfloat16).transpose(2, 0, 1, 3).reshape(slots, query_count)
    )

    parts = jnp.concatenate(
        [shortlist // 256, shortlist % 256, positives // 256, positives % 256,
         jnp.ones((query_count, 1), jnp.int32)],
        axis=1,
    ).astype(jnp.bfloat16)
    gathered = jnp.dot(dispatch, parts, preferred_element_type=jnp.float32)
    k_hi = gathered[:, :shortlist_size]
    k_lo = gathered[:, shortlist_size : 2 * shortlist_size]
    p_base = 2 * shortlist_size
    slot_list = (k_hi * 256 + k_lo).astype(jnp.int32)
    raw = (
        gathered[:, p_base : p_base + positive_count] * 256
        + gathered[:, p_base + positive_count : p_base + 2 * positive_count]
    ).astype(jnp.int32)
    occupied = gathered[:, p_base + 2 * positive_count :] > 0.5
    row = jnp.arange(slots, dtype=jnp.int32)[:, None]
    slot_cluster = row // CAP
    slot_k = jnp.sum(
        jnp.where(slot_list == slot_cluster, jnp.arange(shortlist_size, dtype=jnp.int32), 0),
        axis=1, keepdims=True,
    )
    offsets = raw - slot_k * block_labels
    inside = (offsets >= 0) & (offsets < block_labels) & occupied
    local_positive = jnp.where(inside, offsets, -1).astype(jnp.int32)

    by_cluster = jnp.transpose(label_weight, (1, 0, 2))
    rows_per_cluster = CAP * devices
    dispatch = dispatch.reshape(devices, per_dst, query_count)
    query_grad = jnp.zeros((query_count, width), jnp.float32)
    grad = None
    first = 0
    for count in CHUNKS:
        rows = count * CAP
        part = dispatch[:, first * CAP : first * CAP + rows, :].reshape(devices * rows, query_count)
        outgoing = jnp.dot(part, queries, preferred_element_type=jnp.float32).astype(jnp.bfloat16)
        incoming = lax.all_to_all(
            outgoing.reshape(devices, rows, width), AXES, split_axis=0, concat_axis=0, tiled=True
        )
        if first == 0:
            local_positive, incoming = lax.optimization_barrier((local_positive, incoming))
            incoming_pos = lax.all_to_all(
                local_positive.reshape(devices, per_dst, positive_count),
                AXES, split_axis=0, concat_axis=0, tiled=True,
            )
            incoming_pos = incoming_pos.transpose(1, 0, 2).reshape(slots, positive_count)
        incoming = incoming.transpose(1, 0, 2).reshape(devices * rows, width)
        operands = [incoming, incoming_pos, by_cluster]
        aliases = {}
        if grad is not None:
            operands.append(grad)
            aliases = {3: 0}
        grad, row_grads = pl.pallas_call(
            cluster_kernel,
            grid=(count,),
            in_specs=[
                pl.BlockSpec((rows_per_cluster, width), lambda c: (c, 0)),
                pl.BlockSpec((rows_per_cluster, positive_count), lambda c, f=first: (c + f, 0)),
                pl.BlockSpec((1, block_labels, width), lambda c, f=first: (c + f, 0, 0)),
            ] + ([pl.BlockSpec(memory_space=pl.ANY)] if aliases else []),
            out_specs=[
                pl.BlockSpec((1, block_labels, width), lambda c, f=first: (c + f, 0, 0)),
                pl.BlockSpec((rows_per_cluster, width), lambda c: (c, 0)),
            ],
            out_shape=[
                jax.ShapeDtypeStruct((local_clusters, block_labels, width), jnp.float32),
                jax.ShapeDtypeStruct((devices * rows, width), jnp.bfloat16),
            ],
            input_output_aliases=aliases,
            compiler_params=pltpu.CompilerParams(vmem_limit_bytes=48 * 1024 * 1024),
            cost_estimate=pl.CostEstimate(
                flops=6 * devices * rows * block_labels * width,
                transcendentals=devices * rows * block_labels,
                bytes_accessed=4 * devices * rows * width + count * block_labels * width * 6,
            ),
        )(*operands)
        row_grads = row_grads.reshape(rows, devices, width).transpose(1, 0, 2)
        returned = lax.all_to_all(
            row_grads, AXES, split_axis=0, concat_axis=0, tiled=True
        ).reshape(devices * rows, width)
        query_grad = query_grad + lax.dot_general(
            part, returned, (((0,), (0,)), ((), ())), preferred_element_type=jnp.float32
        )
        first += count
    weight_grad = jnp.transpose(grad, (1, 0, 2))
    return (query_grad, weight_grad)


def solution(mesh):
    in_specs = (
        P(AXES, None),
        P(),
        P(),
        P(AXES, None),
        P(AXES, None),
        P(None, AXES, None),
    )
    out_specs = (P(AXES, None), P(None, AXES, None))
    return jax.shard_map(step, mesh=mesh, in_specs=in_specs, out_specs=out_specs, check_vma=False)
```

```python
import jax
import jax.numpy as jnp
from jax import lax
from jax.sharding import PartitionSpec as P
from jax.experimental import pallas as pl
from jax.experimental.pallas import tpu as pltpu

CAP = 6
CHUNKS = (8, 4)
AXES = ("row", "col")


def encode(pooled, enc_weight, norm_gain):
    projected = jnp.dot(pooled, enc_weight, preferred_element_type=jnp.float32)
    average = jnp.mean(projected, axis=-1, keepdims=True)
    centred = projected - average
    spread = jnp.mean(centred * centred, axis=-1, keepdims=True)
    return (centred * lax.rsqrt(spread + 1e-05) * norm_gain).astype(jnp.bfloat16)


def cluster_kernel(incoming_ref, positive_ref, weight_ref, *refs):
    grad_ref, rows_ref = refs[-2:]
    block = weight_ref[0]
    x = incoming_ref[...]
    scores = lax.dot_general(
        x, block, (((1,), (1,)), ((), ())), preferred_element_type=jnp.float32
    )
    labels = lax.broadcasted_iota(jnp.int32, (1, block.shape[0]), 1)
    marks = positive_ref[...]
    target = marks[:, 0:1] == labels
    for column in range(1, marks.shape[1]):
        target = target | (marks[:, column : column + 1] == labels)
    signal = (jax.nn.sigmoid(scores) - target.astype(jnp.float32)).astype(jnp.bfloat16)
    grad_ref[0] = lax.dot_general(
        signal, x, (((0,), (0,)), ((), ())), preferred_element_type=jnp.float32
    )
    rows_ref[...] = jnp.dot(signal, block, preferred_element_type=jnp.float32).astype(jnp.bfloat16)


def step(pooled, enc_weight, norm_gain, shortlist, positives, label_weight):
    queries = encode(pooled, enc_weight, norm_gain)
    devices = lax.axis_size("row") * lax.axis_size("col")
    query_count, width = queries.shape
    block_labels, local_clusters, _ = label_weight.shape
    shortlist_size = shortlist.shape[1]
    positive_count = positives.shape[1]
    clusters = devices * local_clusters
    slots = clusters * CAP
    per_dst = local_clusters * CAP

    local_of = jnp.arange(local_clusters, dtype=jnp.int32)[:, None]
    device_of = jnp.arange(devices, dtype=jnp.int32)[None, :]
    cluster_id = (device_of * local_clusters + local_of).reshape(clusters)
    member = jnp.any(shortlist.T[:, None, :] == cluster_id[None, :, None], axis=0)
    earlier = (
        jnp.arange(query_count, dtype=jnp.int32)[:, None]
        < jnp.arange(query_count, dtype=jnp.int32)[None, :]
    ).astype(jnp.bfloat16)
    rank = jnp.dot(member.astype(jnp.bfloat16), earlier, preferred_element_type=jnp.float32)
    level = jnp.where(member, rank, float(CAP + 1)).astype(jnp.bfloat16)
    level = level.reshape(local_clusters, 1, devices, query_count)
    slot_rank = jnp.arange(CAP, dtype=jnp.int32).astype(jnp.bfloat16)[None, :, None, None]
    dispatch = (
        (level == slot_rank).astype(jnp.bfloat16).transpose(2, 0, 1, 3).reshape(slots, query_count)
    )

    parts = jnp.concatenate(
        [shortlist // 256, shortlist % 256, positives // 256, positives % 256,
         jnp.ones((query_count, 1), jnp.int32)],
        axis=1,
    ).astype(jnp.bfloat16)
    gathered = jnp.dot(dispatch, parts, preferred_element_type=jnp.float32)
    k_hi = gathered[:, :shortlist_size]
    k_lo = gathered[:, shortlist_size : 2 * shortlist_size]
    p_base = 2 * shortlist_size
    slot_list = (k_hi * 256 + k_lo).astype(jnp.int32)
    raw = (
        gathered[:, p_base : p_base + positive_count] * 256
        + gathered[:, p_base + positive_count : p_base + 2 * positive_count]
    ).astype(jnp.int32)
    occupied = gathered[:, p_base + 2 * positive_count :] > 0.5
    row = jnp.arange(slots, dtype=jnp.int32)[:, None]
    slot_cluster = row // CAP
    slot_k = jnp.sum(
        jnp.where(slot_list == slot_cluster, jnp.arange(shortlist_size, dtype=jnp.int32), 0),
        axis=1, keepdims=True,
    )
    offsets = raw - slot_k * block_labels
    inside = (offsets >= 0) & (offsets < block_labels) & occupied
    local_positive = jnp.where(inside, offsets, -1).astype(jnp.int32)

    by_cluster = jnp.transpose(label_weight, (1, 0, 2))
    rows_per_cluster = CAP * devices
    query_grad = jnp.zeros((query_count, width), jnp.float32)
    grad = None
    first = 0
    for count in CHUNKS:
        rows = count * CAP
        part = (
            (level[first : first + count] == slot_rank)
            .astype(jnp.bfloat16)
            .transpose(2, 0, 1, 3)
            .reshape(devices * rows, query_count)
        )
        outgoing = jnp.dot(part, queries, preferred_element_type=jnp.float32).astype(jnp.bfloat16)
        incoming = lax.all_to_all(
            outgoing.reshape(devices, rows, width), AXES, split_axis=0, concat_axis=0, tiled=True
        )
        if first == 0:
            local_positive, incoming = lax.optimization_barrier((local_positive, incoming))
            incoming_pos = lax.all_to_all(
                local_positive.reshape(devices, per_dst, positive_count),
                AXES, split_axis=0, concat_axis=0, tiled=True,
            )
            incoming_pos = incoming_pos.transpose(1, 0, 2).reshape(slots, positive_count)
        incoming = incoming.transpose(1, 0, 2).reshape(devices * rows, width)
        operands = [incoming, incoming_pos, by_cluster]
        aliases = {}
        if grad is not None:
            operands.append(grad)
            aliases = {3: 0}
        grad, row_grads = pl.pallas_call(
            cluster_kernel,
            grid=(count,),
            in_specs=[
                pl.BlockSpec((rows_per_cluster, width), lambda c: (c, 0)),
                pl.BlockSpec((rows_per_cluster, positive_count), lambda c, f=first: (c + f, 0)),
                pl.BlockSpec((1, block_labels, width), lambda c, f=first: (c + f, 0, 0)),
            ] + ([pl.BlockSpec(memory_space=pl.ANY)] if aliases else []),
            out_specs=[
                pl.BlockSpec((1, block_labels, width), lambda c, f=first: (c + f, 0, 0)),
                pl.BlockSpec((rows_per_cluster, width), lambda c: (c, 0)),
            ],
            out_shape=[
                jax.ShapeDtypeStruct((local_clusters, block_labels, width), jnp.float32),
                jax.ShapeDtypeStruct((devices * rows, width), jnp.bfloat16),
            ],
            input_output_aliases=aliases,
            compiler_params=pltpu.CompilerParams(vmem_limit_bytes=48 * 1024 * 1024),
            cost_estimate=pl.CostEstimate(
                flops=6 * devices * rows * block_labels * width,
                transcendentals=devices * rows * block_labels,
                bytes_accessed=4 * devices * rows * width + count * block_labels * width * 6,
            ),
        )(*operands)
        row_grads = row_grads.reshape(rows, devices, width).transpose(1, 0, 2)
        returned = lax.all_to_all(
            row_grads, AXES, split_axis=0, concat_axis=0, tiled=True
        ).reshape(devices * rows, width)
        query_grad = query_grad + lax.dot_general(
            part, returned, (((0,), (0,)), ((), ())), preferred_element_type=jnp.float32
        )
        first += count
    weight_grad = jnp.transpose(grad, (1, 0, 2))
    return (query_grad, weight_grad)


def solution(mesh):
    in_specs = (
        P(AXES, None),
        P(),
        P(),
        P(AXES, None),
        P(AXES, None),
        P(None, AXES, None),
    )
    out_specs = (P(AXES, None), P(None, AXES, None))
    return jax.shard_map(step, mesh=mesh, in_specs=in_specs, out_specs=out_specs, check_vma=False)
```
